512 devices in a mesh: section: 8 (over y, core), expert: 64 (over z, x).
Axes of the slice: x: 4, y: 4, z: 16, core: 2. Of those that a mesh axis runs over, the one named last changes fastest.
Arguments:
- tokens: bfloat16 [8, 8192, 2048], P('section', 'expert'), may hold values from -6 to 6
- grad_out: bfloat16 [8, 8192, 2048], P('section', 'expert'), may hold values from -3 to 3
- expert_ids: int32 [8, 8192, 1], P('section', 'expert'), may hold values from 0 to 15; in each aligned block of 128 rows (0 to 127, 128 to 255, ..., all dimensions but the last counted through in order) at most 16 rows name the same one
- route_weight: bfloat16 [8, 8192, 1], P('section', 'expert'), may hold values from 0.25 to 1
- gate_weight: bfloat16 [8, 64, 2048, 256], P('section', 'expert'), may hold values from -0.125 to 0.125
- up_weight: bfloat16 [8, 64, 2048, 256], P('section', 'expert'), may hold values from -0.125 to 0.125
- down_weight: bfloat16 [8, 64, 256, 2048], P('section', 'expert'), may hold values from -0.1875 to 0.1875
Outputs:
- handed_grad: bfloat16 [8, 8192, 2048], P('section', 'expert')
- gate_grad: bfloat16 [8, 8192, 1], P('section', 'expert')
The draws below stay inside these ranges and needn't reach their ends.
Inputs may be any that keep to these rules, and one draw needn't show every extreme that they name: `expert_ids`: among the route rows of one device, at most 16 name the same expert, and in every draw some expert is named by exactly 16 rows of some device.
All inputs are finite; a program needn't handle non-finite values.
Results may differ from the reference program's by a relative error of at most 0.0058.
Values may be sent and summed in bfloat16 or wider, within the bound.
No kernel may reach another device: no remote copies, remote signals or barrier semaphores. Data moves between devices by JAX's collectives and lax.ppermute only.
A program may use at most 64 MiB of HBM per device.

```python
import math
import jax
import jax.numpy as jnp
import numpy as np
from jax import lax

D = 2048
FF = 1024
SPLIT = 4
TOPK = 1
TOK_DEV = 128
SECTIONS = 8
EXPERTS = 16
SHARDS = 64
H_DEV = 256
TOKENS = 8192
CAP = 16


def block_levels(key, shape, shards, low, largest):
    loudness, own = 1.0, jax.random.fold_in(key, 6)
    for dim, shards_of in shards:
        steps = jnp.exp(jax.random.uniform(jax.random.fold_in(own, dim), (shards_of,), jnp.float32, low / len(shards), largest / len(shards)))
        loudness = loudness * jnp.repeat(steps, shape[dim] // shards_of).reshape([-1 if axis == dim else 1 for axis in range(len(shape))])
    return loudness


def routed_block(stream_key, own, number, rows, amount, top, most, lean):
    sequence = jax.random.permutation(stream_key, amount)
    crowded, ordinary = shares(amount, rows * top, most, lean, True), shares(amount, rows * top, most, lean, False)
    places = jnp.arange(amount)

    def named(sizes, offset_by):
        used = int((sizes > 0).sum())
        fixed = max(1, used // 4)
        shifted = fixed + (places - fixed + offset_by * (used - fixed)) % max(1, amount - fixed)
        return jnp.zeros((amount,), jnp.int32).at[sequence[jnp.where(places < fixed, places, shifted)]].set(jnp.asarray(sizes, jnp.int32))

    sizes = jnp.where(number % 4 == 0, named(crowded, number // 4), named(ordinary, number - number // 4 - 1))
    mixed = jax.random.permutation(jax.random.fold_in(own, 3), amount)
    donor, sink = mixed[0:amount // 2 * 2:2], mixed[1:amount // 2 * 2:2]
    room = jnp.minimum(sizes[donor] - 1, most - sizes[sink]) // 2
    room = jnp.where((donor == sequence[0]) | (sink == sequence[0]) | (sizes[sink] == 0), 0, jnp.maximum(room, 0))
    shifted = jax.random.randint(jax.random.fold_in(own, 4), (amount // 2,), 0, 1 << 20) % (room + 1)
    sizes = sizes.at[donor].add(-shifted).at[sink].add(shifted)
    items = jnp.searchsorted(jnp.cumsum(sizes), jnp.arange(rows * top), side="right").astype(jnp.int32)
    table = items.reshape(top, rows).T
    table = table[jax.random.permutation(jax.random.fold_in(own, 1), rows)]
    offset_by = jax.random.randint(jax.random.fold_in(own, 2), (rows, 1), 0, top)
    return jnp.take_along_axis(table, (jnp.arange(top)[None, :] + offset_by) % top, axis=1)


def shares(count, total, reach, lean, full):
    weights = [(1 << 20) // math.isqrt(standing ** lean) + 1 for standing in range(1, count + 1)]
    largest = reach if full else min(reach, max(-(-total // count), total * weights[0] // sum(weights)))
    least = 1 if total - largest >= count - 1 else 0
    given, spare = [largest] + [least] * (count - 1), total - largest - least * (count - 1)
    while spare > 0:
        movable = [i for i in range(1, count) if given[i] < largest] or [i for i in range(1, count) if given[i] < reach]
        mass, left = sum([weights[i] for i in movable]), spare
        for i in movable:
            extra = min(reach - given[i], max(1, left * weights[i] // mass), spare)
            given[i] = given[i] + extra
            spare = spare - extra
    return np.array(given)


def gaussian(rng, extent, deviation, reach, split=(), held_as=jnp.bfloat16):
    values = deviation * jax.random.normal(rng, extent, jnp.float32)
    if split:
        values = values * block_levels(rng, extent, split, -0.22, 0.18)
    return jnp.clip(values, -reach, reach).astype(held_as)


def setup_inputs(seed: int = 0) -> dict:
    keys = jax.random.split(jax.random.key(seed), 8)
    tokens = gaussian(keys[0], (SECTIONS, TOKENS, D), 1.0, 6.0, ((0, 8), (1, 64)))
    grad_out = gaussian(keys[1], (SECTIONS, TOKENS, D), 0.5, 3.0, ((0, 8), (1, 64)))
    expert_ids_keys = jax.random.split(jax.random.fold_in(keys[2], 1), SECTIONS * TOKENS // TOK_DEV)
    expert_ids_turns = jax.random.permutation(jax.random.fold_in(keys[2], 3), SECTIONS * TOKENS // TOK_DEV)
    expert_ids = jax.vmap(lambda own, number: routed_block(jax.random.fold_in(keys[2], 2), own, number, TOK_DEV, EXPERTS, TOPK, CAP, 2))(expert_ids_keys, expert_ids_turns).reshape((SECTIONS, TOKENS, TOPK))
    route_weight = jnp.clip(0.25 + 0.75 * jax.random.uniform(keys[3], (SECTIONS, TOKENS, TOPK), jnp.float32) ** block_levels(keys[3], (SECTIONS, TOKENS, TOPK), ((0, 8), (1, 64)), -0.2, 0.2), 0.25, 1.0).astype(jnp.bfloat16)
    gate_weight = gaussian(keys[4], (SECTIONS, SHARDS, D, H_DEV), D ** -0.5, 0.125, ((0, 8), (1, 64)))
    up_weight = gaussian(keys[5], (SECTIONS, SHARDS, D, H_DEV), D ** -0.5, 0.125, ((0, 8), (1, 64)))
    down_weight = gaussian(keys[6], (SECTIONS, SHARDS, H_DEV, D), FF ** -0.5, 0.1875, ((0, 8), (1, 64)))
    return {"tokens": tokens, "grad_out": grad_out, "expert_ids": expert_ids, "route_weight": route_weight, "gate_weight": gate_weight, "up_weight": up_weight, "down_weight": down_weight}


def shard_terms(rows_x, rows_g, rows_p, w_gate, w_up, w_down):
    gate = jnp.dot(rows_x, w_gate, preferred_element_type=jnp.float32)
    upval = jnp.dot(rows_x, w_up, preferred_element_type=jnp.float32)
    sig = jax.nn.sigmoid(gate)
    act = gate * sig
    hidden = act * upval
    zeta = lax.dot_general(rows_g, w_down, (((1,), (1,)), ((), ())), preferred_element_type=jnp.float32)
    part_p = jnp.sum(hidden * zeta, axis=1).astype(jnp.bfloat16)
    d_hidden = rows_p.astype(jnp.float32)[:, None] * zeta
    d_gate = (d_hidden * upval * sig * (1.0 + gate * (1.0 - sig))).astype(jnp.bfloat16)
    d_up = (d_hidden * act).astype(jnp.bfloat16)
    part_x = lax.dot_general(d_gate, w_gate, (((1,), (1,)), ((), ())), preferred_element_type=jnp.float32)
    part_x = part_x + lax.dot_general(d_up, w_up, (((1,), (1,)), ((), ())), preferred_element_type=jnp.float32)
    return part_x.astype(jnp.bfloat16), part_p


def one_section(inputs):
    x_all, gy_all, ids_all, pw_all, wg_all, wu_all, wd_all = inputs
    devices = TOKENS // TOK_DEV
    rows = TOK_DEV * TOPK
    ids_dev = ids_all.reshape(devices, rows).astype(jnp.int32)
    onehot = (ids_dev[:, :, None] == jnp.arange(EXPERTS, dtype=jnp.int32)[None, None, :]).astype(jnp.int32)
    before = jnp.cumsum(onehot, axis=1) - onehot
    slot = jnp.sum(before * onehot, axis=2).astype(jnp.int32)
    source = jnp.arange(devices, dtype=jnp.int32)[:, None]
    place = (ids_dev * (devices * CAP) + source * CAP + slot).reshape(-1).astype(jnp.int32)
    total_rows = EXPERTS * devices * CAP
    rows_x = jnp.repeat(x_all, TOPK, axis=0)
    rows_g = jnp.repeat(gy_all, TOPK, axis=0)
    buf_x = jnp.zeros((total_rows, D), jnp.bfloat16).at[place].set(rows_x)
    buf_g = jnp.zeros((total_rows, D), jnp.bfloat16).at[place].set(rows_g)
    buf_p = jnp.zeros((total_rows,), jnp.bfloat16).at[place].set(pw_all.reshape(-1))
    buf_x = buf_x.reshape(EXPERTS, devices * CAP, D)
    buf_g = buf_g.reshape(EXPERTS, devices * CAP, D)
    buf_p = buf_p.reshape(EXPERTS, devices * CAP)
    wg_e = wg_all.reshape(EXPERTS, SPLIT, D, H_DEV)
    wu_e = wu_all.reshape(EXPERTS, SPLIT, D, H_DEV)
    wd_e = wd_all.reshape(EXPERTS, SPLIT, H_DEV, D)

    def per_expert(item):
        bx, bg, bp, wge, wue, wde = item
        sum_x = jnp.zeros((devices * CAP, D), jnp.float32)
        sum_p = jnp.zeros((devices * CAP,), jnp.float32)
        for shard in range(SPLIT):
            part_x, part_p = shard_terms(bx, bg, bp, wge[shard], wue[shard], wde[shard])
            sum_x = sum_x + part_x.astype(jnp.float32)
            sum_p = sum_p + part_p.astype(jnp.float32)
        return sum_x.astype(jnp.bfloat16), sum_p.astype(jnp.bfloat16)

    out_x, out_p = lax.map(per_expert, (buf_x, buf_g, buf_p, wg_e, wu_e, wd_e))
    route_x = out_x.reshape(total_rows, D)[place].astype(jnp.float32)
    input_grad = jnp.sum(route_x.reshape(TOKENS, TOPK, D), axis=1).astype(jnp.bfloat16)
    gate_grad = out_p.reshape(total_rows)[place].reshape(TOKENS, TOPK)
    return input_grad, gate_grad


def reference(tokens, grad_out, expert_ids, route_weight, gate_weight, up_weight, down_weight):
    input_grad, gate_grad = lax.map(one_section, (tokens, grad_out, expert_ids, route_weight, gate_weight, up_weight, down_weight))
    handed_grad = jnp.roll(input_grad, -1, axis=0)
    return handed_grad, gate_grad
```

```python
import jax
import jax.numpy as jnp
from jax import lax
from jax.sharding import Mesh
from jax.sharding import PartitionSpec as P

SPLIT = 4
TOPK = 1
CAP = 16
PAD = 128


def from_behind(block, axis, distance):
    devices = range(lax.axis_size(axis))
    route = [((i - distance) % len(devices), i) for i in devices]
    return lax.ppermute(block, axis, route)


def shard_terms(rows_x, rows_g, rows_p, w_gate, w_up, w_down):
    gate = jnp.dot(rows_x, w_gate, preferred_element_type=jnp.float32)
    upval = jnp.dot(rows_x, w_up, preferred_element_type=jnp.float32)
    sig = jax.nn.sigmoid(gate)
    act = gate * sig
    hidden = act * upval
    zeta = lax.dot_general(
        rows_g, w_down, (((1,), (1,)), ((), ())), preferred_element_type=jnp.float32
    )
    part_p = jnp.sum(hidden * zeta, axis=1).astype(jnp.bfloat16)
    d_hidden = rows_p.astype(jnp.float32)[:, None] * zeta
    d_gate = (d_hidden * upval * sig * (1.0 + gate * (1.0 - sig))).astype(jnp.bfloat16)
    d_up = (d_hidden * act).astype(jnp.bfloat16)
    part_x = lax.dot_general(
        d_gate, w_gate, (((1,), (1,)), ((), ())), preferred_element_type=jnp.float32
    )
    part_x = part_x + lax.dot_general(
        d_up, w_up, (((1,), (1,)), ((), ())), preferred_element_type=jnp.float32
    )
    return part_x.astype(jnp.bfloat16), part_p


def pad_column(values, rows):
    col = jnp.zeros((rows, PAD), jnp.bfloat16)
    return col.at[:, 0].set(values.astype(jnp.bfloat16))


def on_device(tokens, grad_out, expert_ids, route_weight, gate_weight, up_weight, down_weight):
    feats = tokens[0]
    grads = grad_out[0]
    route_ids = expert_ids[0].reshape(-1)
    route_w = route_weight[0].reshape(-1)
    w_gate = lax.all_gather(gate_weight[0, 0], "ex")
    w_up = lax.all_gather(up_weight[0, 0], "ex")
    w_down = lax.all_gather(down_weight[0, 0], "ex")
    groups = lax.axis_size("ez")
    tok_count, width = feats.shape
    rows = tok_count * TOPK
    onehot = (route_ids[:, None] == jnp.arange(groups, dtype=jnp.int32)[None, :]).astype(jnp.int32)
    before = jnp.cumsum(onehot, axis=0) - onehot
    slot = jnp.sum(before * onehot, axis=1)
    place = route_ids * CAP + slot
    table = (place[None, :] == jnp.arange(groups * CAP, dtype=jnp.int32)[:, None]).astype(
        jnp.bfloat16
    )
    packed = jnp.concatenate(
        [jnp.repeat(feats, TOPK, axis=0), jnp.repeat(grads, TOPK, axis=0), pad_column(route_w, rows)],
        axis=1,
    )
    send = jnp.dot(table, packed, preferred_element_type=jnp.float32).astype(jnp.bfloat16)
    recv = lax.all_to_all(
        send.reshape(groups, CAP, -1), "ez", split_axis=0, concat_axis=0, tiled=True
    ).reshape(groups * CAP, -1)
    rows_x = recv[:, :width]
    rows_g = recv[:, width : 2 * width]
    rows_p = recv[:, 2 * width]
    sum_x = None
    sum_p = None
    for q in range(w_gate.shape[0]):
        part_x, part_p = shard_terms(rows_x, rows_g, rows_p, w_gate[q], w_up[q], w_down[q])
        if sum_x is None:
            sum_x = part_x.astype(jnp.float32)
            sum_p = part_p.astype(jnp.float32)
        else:
            sum_x = sum_x + part_x.astype(jnp.float32)
            sum_p = sum_p + part_p.astype(jnp.float32)
    reply = jnp.concatenate(
        [sum_x.astype(jnp.bfloat16), pad_column(sum_p.astype(jnp.bfloat16), groups * CAP)], axis=1
    )
    back = lax.all_to_all(
        reply.reshape(groups, CAP, -1), "ez", split_axis=0, concat_axis=0, tiled=True
    ).reshape(groups * CAP, -1)
    picked = jnp.take(back, place, axis=0)
    input_grad = jnp.sum(
        picked[:, :width].astype(jnp.float32).reshape(tok_count, TOPK, width), axis=1
    ).astype(jnp.bfloat16)
    gate_grad = picked[:, width].reshape(tok_count, TOPK)
    handed = from_behind(input_grad, "section", -1)
    return (handed[None], gate_grad[None])


def solution(mesh):
    sections = mesh.shape["section"]
    experts = mesh.shape["expert"]
    grid = mesh.devices.reshape(sections, experts // SPLIT, SPLIT)
    split_mesh = Mesh(grid, ("section", "ez", "ex"))
    spec3 = P("section", ("ez", "ex"), None)
    spec4 = P("section", ("ez", "ex"), None, None)
    in_specs = (spec3, spec3, spec3, spec3, spec4, spec4, spec4)
    out_specs = (spec3, spec3)
    return jax.shard_map(
        on_device, mesh=split_mesh, in_specs=in_specs, out_specs=out_specs, check_vma=False
    )
```

```python
import jax
import jax.numpy as jnp
from jax import lax
from jax.sharding import Mesh
from jax.sharding import PartitionSpec as P

SPLIT = 4
TOPK = 1
CAP = 16
PAD = 128


def from_behind(block, axis, distance):
    devices = range(lax.axis_size(axis))
    route = [((i - distance) % len(devices), i) for i in devices]
    return lax.ppermute(block, axis, route)


def ring_shift(block, axis, step):
    size = lax.axis_size(axis)
    return lax.ppermute(block, axis, [(i, (i + step) % size) for i in range(size)])


def gather_shards(weights, axis):
    left = [ring_shift(w, axis, 1) for w in weights]
    right = [ring_shift(w, axis, -1) for w in weights]
    opposite = []
    for a, b in zip(left, right):
        half = a.shape[0] // 2
        first = ring_shift(a[:half], axis, 1)
        second = ring_shift(b[half:], axis, -1)
        opposite.append(jnp.concatenate([first, second], axis=0))
    return [tuple(weights), tuple(left), tuple(right), tuple(opposite)]


def shard_terms(rows_x, rows_g, rows_p, w_gate, w_up, w_down):
    gate = jnp.dot(rows_x, w_gate, preferred_element_type=jnp.float32)
    upval = jnp.dot(rows_x, w_up, preferred_element_type=jnp.float32)
    sig = jax.nn.sigmoid(gate)
    act = gate * sig
    hidden = act * upval
    zeta = lax.dot_general(
        rows_g, w_down, (((1,), (1,)), ((), ())), preferred_element_type=jnp.float32
    )
    part_p = jnp.sum(hidden * zeta, axis=1).astype(jnp.bfloat16)
    d_hidden = rows_p.astype(jnp.float32)[:, None] * zeta
    d_gate = (d_hidden * upval * sig * (1.0 + gate * (1.0 - sig))).astype(jnp.bfloat16)
    d_up = (d_hidden * act).astype(jnp.bfloat16)
    part_x = lax.dot_general(
        d_gate, w_gate, (((1,), (1,)), ((), ())), preferred_element_type=jnp.float32
    )
    part_x = part_x + lax.dot_general(
        d_up, w_up, (((1,), (1,)), ((), ())), preferred_element_type=jnp.float32
    )
    return part_x.astype(jnp.bfloat16), part_p


def pad_column(values, rows):
    col = jnp.zeros((rows, PAD), jnp.bfloat16)
    return col.at[:, 0].set(values.astype(jnp.bfloat16))


def on_device(tokens, grad_out, expert_ids, route_weight, gate_weight, up_weight, down_weight):
    feats = tokens[0]
    grads = grad_out[0]
    route_ids = expert_ids[0].reshape(-1)
    route_w = route_weight[0].reshape(-1)
    shards = gather_shards((gate_weight[0, 0], up_weight[0, 0], down_weight[0, 0]), "ex")
    groups = lax.axis_size("ez")
    tok_count, width = feats.shape
    rows = tok_count * TOPK
    onehot = (route_ids[:, None] == jnp.arange(groups, dtype=jnp.int32)[None, :]).astype(jnp.int32)
    before = jnp.cumsum(onehot, axis=0) - onehot
    slot = jnp.sum(before * onehot, axis=1)
    place = route_ids * CAP + slot
    table = (place[None, :] == jnp.arange(groups * CAP, dtype=jnp.int32)[:, None]).astype(
        jnp.bfloat16
    )
    packed = jnp.concatenate(
        [jnp.repeat(feats, TOPK, axis=0), jnp.repeat(grads, TOPK, axis=0), pad_column(route_w, rows)],
        axis=1,
    )
    send = jnp.dot(table, packed, preferred_element_type=jnp.float32).astype(jnp.bfloat16)
    recv = lax.all_to_all(
        send.reshape(groups, CAP, -1), "ez", split_axis=0, concat_axis=0, tiled=True
    ).reshape(groups * CAP, -1)
    rows_x = recv[:, :width]
    rows_g = recv[:, width : 2 * width]
    rows_p = recv[:, 2 * width]
    sum_x = None
    sum_p = None
    for w_gate, w_up, w_down in shards:
        part_x, part_p = shard_terms(rows_x, rows_g, rows_p, w_gate, w_up, w_down)
        if sum_x is None:
            sum_x = part_x.astype(jnp.float32)
            sum_p = part_p.astype(jnp.float32)
        else:
            sum_x = sum_x + part_x.astype(jnp.float32)
            sum_p = sum_p + part_p.astype(jnp.float32)
    reply = jnp.concatenate(
        [sum_x.astype(jnp.bfloat16), pad_column(sum_p.astype(jnp.bfloat16), groups * CAP)], axis=1
    )
    back = lax.all_to_all(
        reply.reshape(groups, CAP, -1), "ez", split_axis=0, concat_axis=0, tiled=True
    ).reshape(groups * CAP, -1)
    picked = jnp.take(back, place, axis=0)
    input_grad = jnp.sum(
        picked[:, :width].astype(jnp.float32).reshape(tok_count, TOPK, width), axis=1
    ).astype(jnp.bfloat16)
    gate_grad = picked[:, width].reshape(tok_count, TOPK)
    handed = from_behind(input_grad, "section", -1)
    return (handed[None], gate_grad[None])


def solution(mesh):
    sections = mesh.shape["section"]
    experts = mesh.shape["expert"]
    grid = mesh.devices.reshape(sections, experts // SPLIT, SPLIT)
    split_mesh = Mesh(grid, ("section", "ez", "ex"))
    spec3 = P("section", ("ez", "ex"), None)
    spec4 = P("section", ("ez", "ex"), None, None)
    in_specs = (spec3, spec3, spec3, spec3, spec4, spec4, spec4)
    out_specs = (spec3, spec3)
    return jax.shard_map(
        on_device, mesh=split_mesh, in_specs=in_specs, out_specs=out_specs, check_vma=False
    )
```

```python
import jax
import jax.numpy as jnp
from jax import lax
from jax.sharding import Mesh
from jax.sharding import PartitionSpec as P


SPLIT = 4
TOPK = 1
CAP = 16
PAD = 128
CHUNKS = 2


def from_behind(block, axis, distance):
    devices = range(lax.axis_size(axis))
    route = [((i - distance) % len(devices), i) for i in devices]
    return lax.ppermute(block, axis, route)


def ring_shift(block, axis, step):
    size = lax.axis_size(axis)
    return lax.ppermute(block, axis, [(i, (i + step) % size) for i in range(size)])


def gather_shards(weights, axis):
    left = [ring_shift(w, axis, 1) for w in weights]
    right = [ring_shift(w, axis, -1) for w in weights]
    opposite = []
    for a, b in zip(left, right):
        half = a.shape[0] // 2
        first = ring_shift(a[:half], axis, 1)
        second = ring_shift(b[half:], axis, -1)
        opposite.append(jnp.concatenate([first, second], axis=0))
    return [tuple(weights), tuple(left), tuple(right), tuple(opposite)]


def shard_terms(rows_x, rows_g, rows_p, w_gate, w_up, w_down):
    gate = jnp.dot(rows_x, w_gate, preferred_element_type=jnp.float32)
    upval = jnp.dot(rows_x, w_up, preferred_element_type=jnp.float32)
    sig = jax.nn.sigmoid(gate)
    act = gate * sig
    hidden = act * upval
    zeta = lax.dot_general(
        rows_g, w_down, (((1,), (1,)), ((), ())), preferred_element_type=jnp.float32
    )
    part_p = jnp.sum(hidden * zeta, axis=1).astype(jnp.bfloat16)
    d_hidden = rows_p.astype(jnp.float32)[:, None] * zeta
    d_gate = (d_hidden * upval * sig * (1.0 + gate * (1.0 - sig))).astype(jnp.bfloat16)
    d_up = (d_hidden * act).astype(jnp.bfloat16)
    part_x = lax.dot_general(
        d_gate, w_gate, (((1,), (1,)), ((), ())), preferred_element_type=jnp.float32
    )
    part_x = part_x + lax.dot_general(
        d_up, w_up, (((1,), (1,)), ((), ())), preferred_element_type=jnp.float32
    )
    return part_x.astype(jnp.bfloat16), part_p


def pad_column(values, rows):
    col = jnp.zeros((rows, PAD), jnp.bfloat16)
    return col.at[:, 0].set(values.astype(jnp.bfloat16))


def chunk_pass(c, chunk, groups, width, place, packed, shards):
    wanted = (
        jnp.arange(groups, dtype=jnp.int32)[:, None] * CAP
        + c * chunk
        + jnp.arange(chunk, dtype=jnp.int32)[None, :]
    ).reshape(-1)
    table = (place[None, :] == wanted[:, None]).astype(jnp.bfloat16)
    send = jnp.dot(table, packed, preferred_element_type=jnp.float32).astype(jnp.bfloat16)
    recv = lax.all_to_all(
        send.reshape(groups, chunk, -1), "ez", split_axis=0, concat_axis=0, tiled=True
    ).reshape(groups * chunk, -1)
    rows_x = recv[:, :width]
    rows_g = recv[:, width : 2 * width]
    rows_p = recv[:, 2 * width]
    sum_x = None
    sum_p = None
    for w_gate, w_up, w_down in shards:
        part_x, part_p = shard_terms(rows_x, rows_g, rows_p, w_gate, w_up, w_down)
        if sum_x is None:
            sum_x = part_x.astype(jnp.float32)
            sum_p = part_p.astype(jnp.float32)
        else:
            sum_x = sum_x + part_x.astype(jnp.float32)
            sum_p = sum_p + part_p.astype(jnp.float32)
    reply = jnp.concatenate(
        [sum_x.astype(jnp.bfloat16), pad_column(sum_p.astype(jnp.bfloat16), groups * chunk)],
        axis=1,
    )
    return lax.all_to_all(
        reply.reshape(groups, chunk, -1), "ez", split_axis=0, concat_axis=0, tiled=True
    )


def device_body(tokens, grad_out, expert_ids, route_weight, gate_weight, up_weight, down_weight):
    feats = tokens[0]
    grads = grad_out[0]
    route_ids = expert_ids[0].reshape(-1)
    route_w = route_weight[0].reshape(-1)
    shards = gather_shards((gate_weight[0, 0], up_weight[0, 0], down_weight[0, 0]), "ex")
    groups = lax.axis_size("ez")
    tok_count, width = feats.shape
    rows = tok_count * TOPK
    onehot = (route_ids[:, None] == jnp.arange(groups, dtype=jnp.int32)[None, :]).astype(jnp.int32)
    before = jnp.cumsum(onehot, axis=0) - onehot
    slot = jnp.sum(before * onehot, axis=1)
    place = route_ids * CAP + slot
    packed = jnp.concatenate(
        [jnp.repeat(feats, TOPK, axis=0), jnp.repeat(grads, TOPK, axis=0), pad_column(route_w, rows)],
        axis=1,
    )
    chunk = CAP // CHUNKS
    replies = []
    for c in range(CHUNKS):
        replies.append(chunk_pass(c, chunk, groups, width, place, packed, shards))
    back = jnp.concatenate(replies, axis=1).reshape(groups * CAP, -1)
    picked = jnp.take(back, place, axis=0)
    input_grad = jnp.sum(
        picked[:, :width].astype(jnp.float32).reshape(tok_count, TOPK, width), axis=1
    ).astype(jnp.bfloat16)
    gate_grad = picked[:, width].reshape(tok_count, TOPK)
    handed = from_behind(input_grad, "section", -1)
    return (handed[None], gate_grad[None])


def solution(mesh):
    sections = mesh.shape["section"]
    experts = mesh.shape["expert"]
    grid = mesh.devices.reshape(sections, experts // SPLIT, SPLIT)
    split_mesh = Mesh(grid, ("section", "ez", "ex"))
    spec3 = P("section", ("ez", "ex"), None)
    spec4 = P("section", ("ez", "ex"), None, None)
    in_specs = (spec3, spec3, spec3, spec3, spec4, spec4, spec4)
    out_specs = (spec3, spec3)
    return jax.shard_map(
        device_body, mesh=split_mesh, in_specs=in_specs, out_specs=out_specs, check_vma=False
    )
```

```python
import jax
import jax.numpy as jnp
from jax import lax
from jax.sharding import Mesh
from jax.sharding import PartitionSpec as P

SPLIT = 4
TOPK = 1
CAP = 16
PAD = 128


def from_behind(block, axis, distance):
    devices = range(lax.axis_size(axis))
    route = [((i - distance) % len(devices), i) for i in devices]
    return lax.ppermute(block, axis, route)


def ring_shift(block, axis, step):
    size = lax.axis_size(axis)
    return lax.ppermute(block, axis, [(i, (i + step) % size) for i in range(size)])


def gather_shards(weights, axis):
    left = [ring_shift(w, axis, 1) for w in weights]
    right = [ring_shift(w, axis, -1) for w in weights]
    opposite = []
    for a, b in zip(left, right):
        half = a.shape[0] // 2
        first = ring_shift(a[:half], axis, 1)
        second = ring_shift(b[half:], axis, -1)
        opposite.append(jnp.concatenate([first, second], axis=0))
    return [tuple(weights), tuple(left), tuple(right), tuple(opposite)]


def shard_terms(rows_x, rows_g, rows_p, w_gate, w_up, w_down):
    gate = jnp.dot(rows_x, w_gate, preferred_element_type=jnp.float32)
    upval = jnp.dot(rows_x, w_up, preferred_element_type=jnp.float32)
    sig = jax.nn.sigmoid(gate)
    act = gate * sig
    hidden = act * upval
    zeta = lax.dot_general(
        rows_g, w_down, (((1,), (1,)), ((), ())), preferred_element_type=jnp.float32
    )
    part_p = jnp.sum(hidden * zeta, axis=1).astype(jnp.bfloat16)
    d_hidden = rows_p.astype(jnp.float32)[:, None] * zeta
    d_gate = (d_hidden * upval * sig * (1.0 + gate * (1.0 - sig))).astype(jnp.bfloat16)
    d_up = (d_hidden * act).astype(jnp.bfloat16)
    part_x = lax.dot_general(
        d_gate, w_gate, (((1,), (1,)), ((), ())), preferred_element_type=jnp.float32
    )
    part_x = part_x + lax.dot_general(
        d_up, w_up, (((1,), (1,)), ((), ())), preferred_element_type=jnp.float32
    )
    return part_x.astype(jnp.bfloat16), part_p


def stacked_terms(rows_x, rows_g, rows_p, w_gate, w_up, w_down):
    gate = lax.dot_general(rows_x, w_gate, (((1,), (1,)), ((), ())), preferred_element_type=jnp.float32)
    upval = lax.dot_general(rows_x, w_up, (((1,), (1,)), ((), ())), preferred_element_type=jnp.float32)
    zeta = lax.dot_general(rows_g, w_down, (((1,), (2,)), ((), ())), preferred_element_type=jnp.float32)
    sig = jax.nn.sigmoid(gate)
    act = gate * sig
    hidden = act * upval
    part_p = jnp.sum(hidden * zeta, axis=2).astype(jnp.bfloat16)
    d_hidden = rows_p.astype(jnp.float32)[:, None, None] * zeta
    d_gate = (d_hidden * upval * sig * (1.0 + gate * (1.0 - sig))).astype(jnp.bfloat16)
    d_up = (d_hidden * act).astype(jnp.bfloat16)
    part_x = lax.dot_general(d_gate, w_gate, (((2,), (2,)), ((1,), (0,))), preferred_element_type=jnp.float32)
    part_x = part_x + lax.dot_general(d_up, w_up, (((2,), (2,)), ((1,), (0,))), preferred_element_type=jnp.float32)
    sum_x = jnp.sum(part_x.astype(jnp.bfloat16).astype(jnp.float32), axis=0)
    sum_p = jnp.sum(part_p.astype(jnp.float32), axis=1)
    return sum_x.astype(jnp.bfloat16), sum_p.astype(jnp.bfloat16)


def pad_column(values, rows):
    col = jnp.zeros((rows, PAD), jnp.bfloat16)
    return col.at[:, 0].set(values.astype(jnp.bfloat16))


def on_device(tokens, grad_out, expert_ids, route_weight, gate_weight, up_weight, down_weight):
    feats = tokens[0]
    grads = grad_out[0]
    route_ids = expert_ids[0].reshape(-1)
    route_w = route_weight[0].reshape(-1)
    shards = gather_shards((gate_weight[0, 0], up_weight[0, 0], down_weight[0, 0]), "ex")
    groups = lax.axis_size("ez")
    tok_count, width = feats.shape
    rows = tok_count * TOPK
    onehot = (route_ids[:, None] == jnp.arange(groups, dtype=jnp.int32)[None, :]).astype(jnp.int32)
    before = jnp.cumsum(onehot, axis=0) - onehot
    slot = jnp.sum(before * onehot, axis=1)
    place = route_ids * CAP + slot
    table = (place[None, :] == jnp.arange(groups * CAP, dtype=jnp.int32)[:, None]).astype(
        jnp.bfloat16
    )
    packed = jnp.concatenate(
        [jnp.repeat(feats, TOPK, axis=0), jnp.repeat(grads, TOPK, axis=0), pad_column(route_w, rows)],
        axis=1,
    )
    send = jnp.dot(table, packed, preferred_element_type=jnp.float32).astype(jnp.bfloat16)
    recv = lax.all_to_all(
        send.reshape(groups, CAP, -1), "ez", split_axis=0, concat_axis=0, tiled=True
    ).reshape(groups * CAP, -1)
    rows_x = recv[:, :width]
    rows_g = recv[:, width : 2 * width]
    rows_p = recv[:, 2 * width]
    w_gate = jnp.stack([w[0] for w in shards])
    w_up = jnp.stack([w[1] for w in shards])
    w_down = jnp.stack([w[2] for w in shards])
    sum_x, sum_p = stacked_terms(rows_x, rows_g, rows_p, w_gate, w_up, w_down)
    reply = jnp.concatenate([sum_x, pad_column(sum_p, groups * CAP)], axis=1)
    back = lax.all_to_all(
        reply.reshape(groups, CAP, -1), "ez", split_axis=0, concat_axis=0, tiled=True
    ).reshape(groups * CAP, -1)
    picked = jnp.take(back, place, axis=0)
    input_grad = jnp.sum(
        picked[:, :width].astype(jnp.float32).reshape(tok_count, TOPK, width), axis=1
    ).astype(jnp.bfloat16)
    gate_grad = picked[:, width].reshape(tok_count, TOPK)
    handed = from_behind(input_grad, "section", -1)
    return (handed[None], gate_grad[None])


def solution(mesh):
    sections = mesh.shape["section"]
    experts = mesh.shape["expert"]
    grid = mesh.devices.reshape(sections, experts // SPLIT, SPLIT)
    split_mesh = Mesh(grid, ("section", "ez", "ex"))
    spec3 = P("section", ("ez", "ex"), None)
    spec4 = P("section", ("ez", "ex"), None, None)
    in_specs = (spec3, spec3, spec3, spec3, spec4, spec4, spec4)
    out_specs = (spec3, spec3)
    return jax.shard_map(
        on_device, mesh=split_mesh, in_specs=in_specs, out_specs=out_specs, check_vma=False
    )
```

```python
import jax
import jax.numpy as jnp
from jax import lax
from jax.sharding import Mesh
from jax.sharding import PartitionSpec as P

SPLIT = 4
TOPK = 1
CAP = 16
PAD = 128


def from_behind(block, axis, distance):
    devices = range(lax.axis_size(axis))
    route = [((i - distance) % len(devices), i) for i in devices]
    return lax.ppermute(block, axis, route)


def ring_shift(block, axis, step):
    size = lax.axis_size(axis)
    return lax.ppermute(block, axis, [(i, (i + step) % size) for i in range(size)])


def gather_shards(weights, axis):
    w_gate, w_up, w_down = weights
    rows, hid = w_gate.shape
    own = jnp.concatenate([w_gate, w_up, w_down.reshape(rows, hid)], axis=0)
    left = ring_shift(own, axis, 1)
    right = ring_shift(own, axis, -1)
    half = own.shape[0] // 2
    with jax.named_scope("relay"):
        first = ring_shift(left[:half], axis, 1)
        second = ring_shift(right[half:], axis, -1)
    opposite = jnp.concatenate([first, second], axis=0)
    stacked = jnp.stack([own, left, right, opposite])
    return (
        stacked[:, :rows],
        stacked[:, rows : 2 * rows],
        stacked[:, 2 * rows :].reshape(-1, hid, rows),
    )

def shard_terms(rows_x, rows_g, rows_p, w_gate, w_up, w_down):
    gate = jnp.dot(rows_x, w_gate, preferred_element_type=jnp.float32)
    upval = jnp.dot(rows_x, w_up, preferred_element_type=jnp.float32)
    sig = jax.nn.sigmoid(gate)
    act = gate * sig
    hidden = act * upval
    zeta = lax.dot_general(
        rows_g, w_down, (((1,), (1,)), ((), ())), preferred_element_type=jnp.float32
    )
    part_p = jnp.sum(hidden * zeta, axis=1).astype(jnp.bfloat16)
    d_hidden = rows_p.astype(jnp.float32)[:, None] * zeta
    d_gate = (d_hidden * upval * sig * (1.0 + gate * (1.0 - sig))).astype(jnp.bfloat16)
    d_up = (d_hidden * act).astype(jnp.bfloat16)
    part_x = lax.dot_general(
        d_gate, w_gate, (((1,), (1,)), ((), ())), preferred_element_type=jnp.float32
    )
    part_x = part_x + lax.dot_general(
        d_up, w_up, (((1,), (1,)), ((), ())), preferred_element_type=jnp.float32
    )
    return part_x.astype(jnp.bfloat16), part_p


def stacked_terms(rows_x, rows_g, rows_p, w_gate, w_up, w_down):
    gate = lax.dot_general(rows_x, w_gate, (((1,), (1,)), ((), ())), preferred_element_type=jnp.float32)
    upval = lax.dot_general(rows_x, w_up, (((1,), (1,)), ((), ())), preferred_element_type=jnp.float32)
    zeta = lax.dot_general(rows_g, w_down, (((1,), (2,)), ((), ())), preferred_element_type=jnp.float32)
    sig = jax.nn.sigmoid(gate)
    act = gate * sig
    hidden = act * upval
    part_p = jnp.sum(hidden * zeta, axis=2).astype(jnp.bfloat16)
    d_hidden = rows_p.astype(jnp.float32)[:, None, None] * zeta
    d_gate = (d_hidden * upval * sig * (1.0 + gate * (1.0 - sig))).astype(jnp.bfloat16)
    d_up = (d_hidden * act).astype(jnp.bfloat16)
    part_x = lax.dot_general(d_gate, w_gate, (((2,), (2,)), ((1,), (0,))), preferred_element_type=jnp.float32)
    part_x = part_x + lax.dot_general(d_up, w_up, (((2,), (2,)), ((1,), (0,))), preferred_element_type=jnp.float32)
    sum_x = jnp.sum(part_x.astype(jnp.bfloat16).astype(jnp.float32), axis=0)
    sum_p = jnp.sum(part_p.astype(jnp.float32), axis=1)
    return sum_x.astype(jnp.bfloat16), sum_p.astype(jnp.bfloat16)


def pad_column(values, rows):
    col = jnp.zeros((rows, PAD), jnp.bfloat16)
    return col.at[:, 0].set(values.astype(jnp.bfloat16))


def on_device(tokens, grad_out, expert_ids, route_weight, gate_weight, up_weight, down_weight):
    feats = tokens[0]
    grads = grad_out[0]
    route_ids = expert_ids[0].reshape(-1)
    route_w = route_weight[0].reshape(-1)
    shards = gather_shards((gate_weight[0, 0], up_weight[0, 0], down_weight[0, 0]), "ex")
    groups = lax.axis_size("ez")
    tok_count, width = feats.shape
    rows = tok_count * TOPK
    onehot = (route_ids[:, None] == jnp.arange(groups, dtype=jnp.int32)[None, :]).astype(jnp.int32)
    before = jnp.cumsum(onehot, axis=0) - onehot
    slot = jnp.sum(before * onehot, axis=1)
    place = route_ids * CAP + slot
    table = (place[None, :] == jnp.arange(groups * CAP, dtype=jnp.int32)[:, None]).astype(
        jnp.bfloat16
    )
    packed = jnp.concatenate(
        [jnp.repeat(feats, TOPK, axis=0), jnp.repeat(grads, TOPK, axis=0), pad_column(route_w, rows)],
        axis=1,
    )
    send = jnp.dot(table, packed, preferred_element_type=jnp.float32).astype(jnp.bfloat16)
    recv = lax.all_to_all(
        send.reshape(groups, CAP, -1), "ez", split_axis=0, concat_axis=0, tiled=True
    ).reshape(groups * CAP, -1)
    rows_x = recv[:, :width]
    rows_g = recv[:, width : 2 * width]
    rows_p = recv[:, 2 * width]
    w_gate, w_up, w_down = shards
    sum_x, sum_p = stacked_terms(rows_x, rows_g, rows_p, w_gate, w_up, w_down)
    reply = jnp.concatenate([sum_x, pad_column(sum_p, groups * CAP)], axis=1)
    back = lax.all_to_all(
        reply.reshape(groups, CAP, -1), "ez", split_axis=0, concat_axis=0, tiled=True
    ).reshape(groups * CAP, -1)
    picked = jnp.take(back, place, axis=0)
    input_grad = jnp.sum(
        picked[:, :width].astype(jnp.float32).reshape(tok_count, TOPK, width), axis=1
    ).astype(jnp.bfloat16)
    gate_grad = picked[:, width].reshape(tok_count, TOPK)
    handed = from_behind(input_grad, "section", -1)
    return (handed[None], gate_grad[None])


def solution(mesh):
    sections = mesh.shape["section"]
    experts = mesh.shape["expert"]
    grid = mesh.devices.reshape(sections, experts // SPLIT, SPLIT)
    split_mesh = Mesh(grid, ("section", "ez", "ex"))
    spec3 = P("section", ("ez", "ex"), None)
    spec4 = P("section", ("ez", "ex"), None, None)
    in_specs = (spec3, spec3, spec3, spec3, spec4, spec4, spec4)
    out_specs = (spec3, spec3)
    return jax.shard_map(
        on_device, mesh=split_mesh, in_specs=in_specs, out_specs=out_specs, check_vma=False
    )
```

```python
import jax
import jax.numpy as jnp
from jax import lax
from jax.sharding import Mesh
from jax.sharding import PartitionSpec as P


SPLIT = 4
TOPK = 1
CAP = 16
PAD = 128


def from_behind(block, axis, distance):
    devices = range(lax.axis_size(axis))
    route = [((i - distance) % len(devices), i) for i in devices]
    return lax.ppermute(block, axis, route)


def ring_shift(block, axis, step):
    size = lax.axis_size(axis)
    return lax.ppermute(block, axis, [(i, (i + step) % size) for i in range(size)])


def gather_shards(weights, axis):
    left, right, opposite = [], [], []
    for w in weights:
        a = ring_shift(w, axis, 1)
        b = ring_shift(w, axis, -1)
        half = a.shape[0] // 2
        first = ring_shift(a[:half], axis, 1)
        second = ring_shift(b[half:], axis, -1)
        left.append(a)
        right.append(b)
        opposite.append(jnp.concatenate([first, second], axis=0))
    return [tuple(weights), tuple(left), tuple(right), tuple(opposite)]


def stacked_terms(rows_x, rows_g, rows_p, w_gate, w_up, w_down):
    gate = lax.dot_general(rows_x, w_gate, (((1,), (1,)), ((), ())), preferred_element_type=jnp.float32)
    upval = lax.dot_general(rows_x, w_up, (((1,), (1,)), ((), ())), preferred_element_type=jnp.float32)
    zeta = lax.dot_general(rows_g, w_down, (((1,), (2,)), ((), ())), preferred_element_type=jnp.float32)
    sig = jax.nn.sigmoid(gate)
    act = gate * sig
    hidden = act * upval
    part_p = jnp.sum(hidden * zeta, axis=2).astype(jnp.bfloat16)
    d_hidden = rows_p.astype(jnp.float32)[:, None, None] * zeta
    d_gate = (d_hidden * upval * sig * (1.0 + gate * (1.0 - sig))).astype(jnp.bfloat16)
    d_up = (d_hidden * act).astype(jnp.bfloat16)
    part_x = lax.dot_general(d_gate, w_gate, (((2,), (2,)), ((1,), (0,))), preferred_element_type=jnp.float32)
    part_x = part_x + lax.dot_general(d_up, w_up, (((2,), (2,)), ((1,), (0,))), preferred_element_type=jnp.float32)
    sum_x = jnp.sum(part_x.astype(jnp.bfloat16).astype(jnp.float32), axis=0)
    sum_p = jnp.sum(part_p.astype(jnp.float32), axis=1)
    return sum_x.astype(jnp.bfloat16), sum_p.astype(jnp.bfloat16)


def pad_column(values, rows):
    col = jnp.zeros((rows, PAD), jnp.bfloat16)
    return col.at[:, 0].set(values.astype(jnp.bfloat16))


def device_body(tokens, grad_out, expert_ids, route_weight, gate_weight, up_weight, down_weight):
    feats = tokens[0]
    grads = grad_out[0]
    route_ids = expert_ids[0].reshape(-1)
    route_w = route_weight[0].reshape(-1)
    shards = gather_shards((gate_weight[0, 0], up_weight[0, 0], down_weight[0, 0]), "ex")
    groups = lax.axis_size("ez")
    tok_count, width = feats.shape
    rows = tok_count * TOPK
    onehot = (route_ids[:, None] == jnp.arange(groups, dtype=jnp.int32)[None, :]).astype(jnp.int32)
    before = jnp.cumsum(onehot, axis=0) - onehot
    slot = jnp.sum(before * onehot, axis=1)
    place = route_ids * CAP + slot
    table = (place[None, :] == jnp.arange(groups * CAP, dtype=jnp.int32)[:, None]).astype(
        jnp.bfloat16
    )
    packed = jnp.concatenate(
        [jnp.repeat(feats, TOPK, axis=0), jnp.repeat(grads, TOPK, axis=0), pad_column(route_w, rows)],
        axis=1,
    )
    send = jnp.dot(table, packed, preferred_element_type=jnp.float32).astype(jnp.bfloat16)
    recv = lax.all_to_all(
        send.reshape(groups, CAP, -1), "ez", split_axis=0, concat_axis=0, tiled=True
    ).reshape(groups * CAP, -1)
    rows_x = recv[:, :width]
    rows_g = recv[:, width : 2 * width]
    rows_p = recv[:, 2 * width]
    w_gate = jnp.stack([w[0] for w in shards])
    w_up = jnp.stack([w[1] for w in shards])
    w_down = jnp.stack([w[2] for w in shards])
    sum_x, sum_p = stacked_terms(rows_x, rows_g, rows_p, w_gate, w_up, w_down)
    reply = jnp.concatenate([sum_x, pad_column(sum_p, groups * CAP)], axis=1)
    back = lax.all_to_all(
        reply.reshape(groups, CAP, -1), "ez", split_axis=0, concat_axis=0, tiled=True
    ).reshape(groups * CAP, -1)
    picked = jnp.take(back, place, axis=0)
    input_grad = jnp.sum(
        picked[:, :width].astype(jnp.float32).reshape(tok_count, TOPK, width), axis=1
    ).astype(jnp.bfloat16)
    gate_grad = picked[:, width].reshape(tok_count, TOPK)
    handed = from_behind(input_grad, "section", -1)
    return (handed[None], gate_grad[None])


def solution(mesh):
    sections = mesh.shape["section"]
    experts = mesh.shape["expert"]
    grid = mesh.devices.reshape(sections, experts // SPLIT, SPLIT)
    split_mesh = Mesh(grid, ("section", "ez", "ex"))
    spec3 = P("section", ("ez", "ex"), None)
    spec4 = P("section", ("ez", "ex"), None, None)
    in_specs = (spec3, spec3, spec3, spec3, spec4, spec4, spec4)
    out_specs = (spec3, spec3)
    return jax.shard_map(device_body, mesh=split_mesh, in_specs=in_specs, out_specs=out_specs, check_vma=False)
```

```python
import jax
import jax.numpy as jnp
from jax import lax
from jax.sharding import Mesh
from jax.sharding import PartitionSpec as P

SPLIT = 4
TOPK = 1
CAP = 16
PAD = 128


def from_behind(block, axis, distance):
    devices = range(lax.axis_size(axis))
    route = [((i - distance) % len(devices), i) for i in devices]
    return lax.ppermute(block, axis, route)


def ring_shift(block, axis, step):
    size = lax.axis_size(axis)
    return lax.ppermute(block, axis, [(i, (i + step) % size) for i in range(size)])


def gather_shards(weights, axis):
    left = [ring_shift(w, axis, 1) for w in weights]
    right = [ring_shift(w, axis, -1) for w in weights]
    opposite = []
    for a, b in zip(left, right):
        half = a.shape[0] // 2
        first = ring_shift(a[:half], axis, 1)
        second = ring_shift(b[half:], axis, -1)
        opposite.append(jnp.concatenate([first, second], axis=0))
    return [tuple(weights), tuple(left), tuple(right), tuple(opposite)]


def shard_terms(rows_x, rows_g, rows_p, w_gate, w_up, w_down):
    gate = jnp.dot(rows_x, w_gate, preferred_element_type=jnp.float32)
    upval = jnp.dot(rows_x, w_up, preferred_element_type=jnp.float32)
    sig = jax.nn.sigmoid(gate)
    act = gate * sig
    hidden = act * upval
    zeta = lax.dot_general(
        rows_g, w_down, (((1,), (1,)), ((), ())), preferred_element_type=jnp.float32
    )
    part_p = jnp.sum(hidden * zeta, axis=1).astype(jnp.bfloat16)
    d_hidden = rows_p.astype(jnp.float32)[:, None] * zeta
    d_gate = (d_hidden * upval * sig * (1.0 + gate * (1.0 - sig))).astype(jnp.bfloat16)
    d_up = (d_hidden * act).astype(jnp.bfloat16)
    part_x = lax.dot_general(
        d_gate, w_gate, (((1,), (1,)), ((), ())), preferred_element_type=jnp.float32
    )
    part_x = part_x + lax.dot_general(
        d_up, w_up, (((1,), (1,)), ((), ())), preferred_element_type=jnp.float32
    )
    return part_x.astype(jnp.bfloat16), part_p


def stacked_terms(rows_x, rows_g, rows_p, w_gate, w_up, w_down):
    gate = lax.dot_general(rows_x, w_gate, (((1,), (1,)), ((), ())), preferred_element_type=jnp.float32)
    upval = lax.dot_general(rows_x, w_up, (((1,), (1,)), ((), ())), preferred_element_type=jnp.float32)
    zeta = lax.dot_general(rows_g, w_down, (((1,), (2,)), ((), ())), preferred_element_type=jnp.float32)
    sig = jax.nn.sigmoid(gate)
    act = gate * sig
    hidden = act * upval
    part_p = jnp.sum(hidden * zeta, axis=2).astype(jnp.bfloat16)
    d_hidden = rows_p.astype(jnp.float32)[:, None, None] * zeta
    d_gate = (d_hidden * upval * sig * (1.0 + gate * (1.0 - sig))).astype(jnp.bfloat16)
    d_up = (d_hidden * act).astype(jnp.bfloat16)
    part_x = lax.dot_general(d_gate, w_gate, (((2,), (2,)), ((1,), (0,))), preferred_element_type=jnp.float32)
    part_x = part_x + lax.dot_general(d_up, w_up, (((2,), (2,)), ((1,), (0,))), preferred_element_type=jnp.float32)
    sum_x = jnp.sum(part_x.astype(jnp.bfloat16).astype(jnp.float32), axis=0)
    sum_p = jnp.sum(part_p.astype(jnp.float32), axis=1)
    return sum_x.astype(jnp.bfloat16), sum_p.astype(jnp.bfloat16)


def pad_column(values, rows):
    col = jnp.zeros((rows, PAD), jnp.bfloat16)
    return col.at[:, 0].set(values.astype(jnp.bfloat16))


def on_device(tokens, grad_out, expert_ids, route_weight, gate_weight, up_weight, down_weight):
    feats = tokens[0]
    grads = grad_out[0]
    route_ids = expert_ids[0].reshape(-1)
    route_w = route_weight[0].reshape(-1)
    shards = gather_shards((gate_weight[0, 0], up_weight[0, 0]), "ex")
    down_all = lax.all_gather(down_weight[0, 0], "ex")
    here = lax.axis_index("ex")
    ring = down_all.shape[0]
    order = (here + jnp.array([0, -1, 1, 2], dtype=jnp.int32)) % ring
    groups = lax.axis_size("ez")
    tok_count, width = feats.shape
    rows = tok_count * TOPK
    onehot = (route_ids[:, None] == jnp.arange(groups, dtype=jnp.int32)[None, :]).astype(jnp.int32)
    before = jnp.cumsum(onehot, axis=0) - onehot
    slot = jnp.sum(before * onehot, axis=1)
    place = route_ids * CAP + slot
    table = (place[None, :] == jnp.arange(groups * CAP, dtype=jnp.int32)[:, None]).astype(
        jnp.bfloat16
    )
    packed = jnp.concatenate(
        [jnp.repeat(feats, TOPK, axis=0), jnp.repeat(grads, TOPK, axis=0), pad_column(route_w, rows)],
        axis=1,
    )
    send = jnp.dot(table, packed, preferred_element_type=jnp.float32).astype(jnp.bfloat16)
    recv = lax.all_to_all(
        send.reshape(groups, CAP, -1), "ez", split_axis=0, concat_axis=0, tiled=True
    ).reshape(groups * CAP, -1)
    rows_x = recv[:, :width]
    rows_g = recv[:, width : 2 * width]
    rows_p = recv[:, 2 * width]
    w_gate = jnp.stack([w[0] for w in shards])
    w_up = jnp.stack([w[1] for w in shards])
    w_down = jnp.take(down_all, order, axis=0)
    sum_x, sum_p = stacked_terms(rows_x, rows_g, rows_p, w_gate, w_up, w_down)
    reply = jnp.concatenate([sum_x, pad_column(sum_p, groups * CAP)], axis=1)
    back = lax.all_to_all(
        reply.reshape(groups, CAP, -1), "ez", split_axis=0, concat_axis=0, tiled=True
    ).reshape(groups * CAP, -1)
    picked = jnp.take(back, place, axis=0)
    input_grad = jnp.sum(
        picked[:, :width].astype(jnp.float32).reshape(tok_count, TOPK, width), axis=1
    ).astype(jnp.bfloat16)
    gate_grad = picked[:, width].reshape(tok_count, TOPK)
    handed = from_behind(input_grad, "section", -1)
    return (handed[None], gate_grad[None])


def solution(mesh):
    sections = mesh.shape["section"]
    experts = mesh.shape["expert"]
    grid = mesh.devices.reshape(sections, experts // SPLIT, SPLIT)
    split_mesh = Mesh(grid, ("section", "ez", "ex"))
    spec3 = P("section", ("ez", "ex"), None)
    spec4 = P("section", ("ez", "ex"), None, None)
    in_specs = (spec3, spec3, spec3, spec3, spec4, spec4, spec4)
    out_specs = (spec3, spec3)
    return jax.shard_map(
        on_device, mesh=split_mesh, in_specs=in_specs, out_specs=out_specs, check_vma=False
    )
```

```python
import jax
import jax.numpy as jnp
from jax import lax
from jax.sharding import Mesh
from jax.sharding import PartitionSpec as P

SPLIT = 4
TOPK = 1
CAP = 16
PAD = 128


def from_behind(block, axis, distance):
    devices = range(lax.axis_size(axis))
    route = [((i - distance) % len(devices), i) for i in devices]
    return lax.ppermute(block, axis, route)


def ring_shift(block, axis, step):
    size = lax.axis_size(axis)
    return lax.ppermute(block, axis, [(i, (i + step) % size) for i in range(size)])


def gather_shards(weights, axis):
    left = [ring_shift(w, axis, 1) for w in weights]
    right = [ring_shift(w, axis, -1) for w in weights]
    opposite = []
    for a, b in zip(left, right):
        half = a.shape[0] // 2
        first = ring_shift(a[:half], axis, 1)
        second = ring_shift(b[half:], axis, -1)
        opposite.append(jnp.concatenate([first, second], axis=0))
    return [tuple(weights), tuple(left), tuple(right), tuple(opposite)]


def shard_terms(rows_x, rows_g, rows_p, w_gate, w_up, w_down):
    gate = jnp.dot(rows_x, w_gate, preferred_element_type=jnp.float32)
    upval = jnp.dot(rows_x, w_up, preferred_element_type=jnp.float32)
    sig = jax.nn.sigmoid(gate)
    act = gate * sig
    hidden = act * upval
    zeta = lax.dot_general(
        rows_g, w_down, (((1,), (1,)), ((), ())), preferred_element_type=jnp.float32
    )
    part_p = jnp.sum(hidden * zeta, axis=1).astype(jnp.bfloat16)
    d_hidden = rows_p.astype(jnp.float32)[:, None] * zeta
    d_gate = (d_hidden * upval * sig * (1.0 + gate * (1.0 - sig))).astype(jnp.bfloat16)
    d_up = (d_hidden * act).astype(jnp.bfloat16)
    part_x = lax.dot_general(
        d_gate, w_gate, (((1,), (1,)), ((), ())), preferred_element_type=jnp.float32
    )
    part_x = part_x + lax.dot_general(
        d_up, w_up, (((1,), (1,)), ((), ())), preferred_element_type=jnp.float32
    )
    return part_x.astype(jnp.bfloat16), part_p


def stacked_terms(rows_x, rows_g, rows_p, w_gate, w_up, w_down):
    gate = lax.dot_general(rows_x, w_gate, (((1,), (1,)), ((), ())), preferred_element_type=jnp.float32)
    upval = lax.dot_general(rows_x, w_up, (((1,), (1,)), ((), ())), preferred_element_type=jnp.float32)
    zeta = lax.dot_general(rows_g, w_down, (((1,), (2,)), ((), ())), preferred_element_type=jnp.float32)
    sig = jax.nn.sigmoid(gate)
    act = gate * sig
    hidden = act * upval
    part_p = jnp.sum(hidden * zeta, axis=2).astype(jnp.bfloat16)
    d_hidden = rows_p.astype(jnp.float32)[:, None, None] * zeta
    d_gate = (d_hidden * upval * sig * (1.0 + gate * (1.0 - sig))).astype(jnp.bfloat16)
    d_up = (d_hidden * act).astype(jnp.bfloat16)
    part_x = lax.dot_general(d_gate, w_gate, (((2,), (2,)), ((1,), (0,))), preferred_element_type=jnp.float32)
    part_x = part_x + lax.dot_general(d_up, w_up, (((2,), (2,)), ((1,), (0,))), preferred_element_type=jnp.float32)
    sum_x = jnp.sum(part_x.astype(jnp.bfloat16).astype(jnp.float32), axis=0)
    sum_p = jnp.sum(part_p.astype(jnp.float32), axis=1)
    return sum_x.astype(jnp.bfloat16), sum_p.astype(jnp.bfloat16)


def pad_column(values, rows):
    col = jnp.zeros((rows, PAD), jnp.bfloat16)
    return col.at[:, 0].set(values.astype(jnp.bfloat16))


def on_device(tokens, grad_out, expert_ids, route_weight, gate_weight, up_weight, down_weight):
    feats = tokens[0]
    grads = grad_out[0]
    route_ids = expert_ids[0].reshape(-1)
    route_w = route_weight[0].reshape(-1)
    shards = gather_shards((gate_weight[0, 0], up_weight[0, 0], down_weight[0, 0]), "ex")
    groups = lax.axis_size("ez")
    tok_count, width = feats.shape
    rows = tok_count * TOPK
    onehot = (route_ids[:, None] == jnp.arange(groups, dtype=jnp.int32)[None, :]).astype(jnp.int32)
    before = jnp.cumsum(onehot, axis=0) - onehot
    slot = jnp.sum(before * onehot, axis=1)
    place = route_ids * CAP + slot
    hit = place[None, :] == jnp.arange(groups * CAP, dtype=jnp.int32)[:, None]
    source = jnp.sum(jnp.where(hit, jnp.arange(rows, dtype=jnp.int32)[None, :], 0), axis=1)
    source = jnp.where(jnp.any(hit, axis=1), source, rows)
    packed = jnp.concatenate(
        [jnp.repeat(feats, TOPK, axis=0), jnp.repeat(grads, TOPK, axis=0), pad_column(route_w, rows)],
        axis=1,
    )
    packed = jnp.concatenate([packed, jnp.zeros((1, packed.shape[1]), jnp.bfloat16)], axis=0)
    send = jnp.take(packed, source, axis=0, mode="clip")
    recv = lax.all_to_all(
        send.reshape(groups, CAP, -1), "ez", split_axis=0, concat_axis=0, tiled=True
    ).reshape(groups * CAP, -1)
    rows_x = recv[:, :width]
    rows_g = recv[:, width : 2 * width]
    rows_p = recv[:, 2 * width]
    w_gate = jnp.stack([w[0] for w in shards])
    w_up = jnp.stack([w[1] for w in shards])
    w_down = jnp.stack([w[2] for w in shards])
    sum_x, sum_p = stacked_terms(rows_x, rows_g, rows_p, w_gate, w_up, w_down)
    reply = jnp.concatenate([sum_x, pad_column(sum_p, groups * CAP)], axis=1)
    back = lax.all_to_all(
        reply.reshape(groups, CAP, -1), "ez", split_axis=0, concat_axis=0, tiled=True
    ).reshape(groups * CAP, -1)
    picked = jnp.take(back, place, axis=0)
    input_grad = jnp.sum(
        picked[:, :width].astype(jnp.float32).reshape(tok_count, TOPK, width), axis=1
    ).astype(jnp.bfloat16)
    gate_grad = picked[:, width].reshape(tok_count, TOPK)
    handed = from_behind(input_grad, "section", -1)
    return (handed[None], gate_grad[None])


def solution(mesh):
    sections = mesh.shape["section"]
    experts = mesh.shape["expert"]
    grid = mesh.devices.reshape(sections, experts // SPLIT, SPLIT)
    split_mesh = Mesh(grid, ("section", "ez", "ex"))
    spec3 = P("section", ("ez", "ex"), None)
    spec4 = P("section", ("ez", "ex"), None, None)
    in_specs = (spec3, spec3, spec3, spec3, spec4, spec4, spec4)
    out_specs = (spec3, spec3)
    return jax.shard_map(
        on_device, mesh=split_mesh, in_specs=in_specs, out_specs=out_specs, check_vma=False
    )
```

```python
import jax
import jax.numpy as jnp
from jax import lax
from jax.sharding import Mesh
from jax.sharding import PartitionSpec as P


SPLIT = 4
TOPK = 1
CAP = 16
PAD = 128


def from_behind(block, axis, distance):
    devices = range(lax.axis_size(axis))
    route = [((i - distance) % len(devices), i) for i in devices]
    return lax.ppermute(block, axis, route)


def ring_shift(block, axis, step):
    size = lax.axis_size(axis)
    return lax.ppermute(block, axis, [(i, (i + step) % size) for i in range(size)])


def gather_shards(weights, axis):
    left = [ring_shift(w, axis, 1) for w in weights]
    right = [ring_shift(w, axis, -1) for w in weights]
    opposite = []
    for k, (a, b) in enumerate(zip(left, right)):
        if k % 2 == 0:
            opposite.append(ring_shift(a, axis, 1))
        else:
            opposite.append(ring_shift(b, axis, -1))
    return [tuple(weights), tuple(left), tuple(right), tuple(opposite)]


def shard_terms(rows_x, rows_g, rows_p, w_gate, w_up, w_down):
    gate = jnp.dot(rows_x, w_gate, preferred_element_type=jnp.float32)
    upval = jnp.dot(rows_x, w_up, preferred_element_type=jnp.float32)
    sig = jax.nn.sigmoid(gate)
    act = gate * sig
    hidden = act * upval
    zeta = lax.dot_general(
        rows_g, w_down, (((1,), (1,)), ((), ())), preferred_element_type=jnp.float32
    )
    part_p = jnp.sum(hidden * zeta, axis=1).astype(jnp.bfloat16)
    d_hidden = rows_p.astype(jnp.float32)[:, None] * zeta
    d_gate = (d_hidden * upval * sig * (1.0 + gate * (1.0 - sig))).astype(jnp.bfloat16)
    d_up = (d_hidden * act).astype(jnp.bfloat16)
    part_x = lax.dot_general(
        d_gate, w_gate, (((1,), (1,)), ((), ())), preferred_element_type=jnp.float32
    )
    part_x = part_x + lax.dot_general(
        d_up, w_up, (((1,), (1,)), ((), ())), preferred_element_type=jnp.float32
    )
    return part_x.astype(jnp.bfloat16), part_p


def stacked_terms(rows_x, rows_g, rows_p, w_gate, w_up, w_down):
    gate = lax.dot_general(rows_x, w_gate, (((1,), (1,)), ((), ())), preferred_element_type=jnp.float32)
    upval = lax.dot_general(rows_x, w_up, (((1,), (1,)), ((), ())), preferred_element_type=jnp.float32)
    zeta = lax.dot_general(rows_g, w_down, (((1,), (2,)), ((), ())), preferred_element_type=jnp.float32)
    sig = jax.nn.sigmoid(gate)
    act = gate * sig
    hidden = act * upval
    part_p = jnp.sum(hidden * zeta, axis=2).astype(jnp.bfloat16)
    d_hidden = rows_p.astype(jnp.float32)[:, None, None] * zeta
    d_gate = (d_hidden * upval * sig * (1.0 + gate * (1.0 - sig))).astype(jnp.bfloat16)
    d_up = (d_hidden * act).astype(jnp.bfloat16)
    part_x = lax.dot_general(d_gate, w_gate, (((2,), (2,)), ((1,), (0,))), preferred_element_type=jnp.float32)
    part_x = part_x + lax.dot_general(d_up, w_up, (((2,), (2,)), ((1,), (0,))), preferred_element_type=jnp.float32)
    sum_x = jnp.sum(part_x.astype(jnp.bfloat16).astype(jnp.float32), axis=0)
    sum_p = jnp.sum(part_p.astype(jnp.float32), axis=1)
    return sum_x, sum_p


def pad_column(values, rows):
    col = jnp.zeros((rows, PAD), jnp.bfloat16)
    return col.at[:, 0].set(values.astype(jnp.bfloat16))


def device_body(tokens, grad_out, expert_ids, route_weight, gate_weight, up_weight, down_weight):
    feats = tokens[0]
    grads = grad_out[0]
    route_ids = expert_ids[0].reshape(-1)
    route_w = route_weight[0].reshape(-1)
    shards = gather_shards((gate_weight[0, 0], up_weight[0, 0], down_weight[0, 0]), "ex")
    groups = lax.axis_size("ez")
    tok_count, width = feats.shape
    rows = tok_count * TOPK
    onehot = (route_ids[:, None] == jnp.arange(groups, dtype=jnp.int32)[None, :]).astype(jnp.int32)
    before = jnp.cumsum(onehot, axis=0) - onehot
    slot = jnp.sum(before * onehot, axis=1)
    place = route_ids * CAP + slot
    table = (place[None, :] == jnp.arange(groups * CAP, dtype=jnp.int32)[:, None]).astype(
        jnp.bfloat16
    )
    packed = jnp.concatenate(
        [jnp.repeat(feats, TOPK, axis=0), jnp.repeat(grads, TOPK, axis=0), pad_column(route_w, rows)],
        axis=1,
    )
    send = jnp.dot(table, packed, preferred_element_type=jnp.float32).astype(jnp.bfloat16)
    recv = lax.all_to_all(
        send.reshape(groups, CAP, -1), "ez", split_axis=0, concat_axis=0, tiled=True
    ).reshape(groups * CAP, -1)
    rows_x = recv[:, :width]
    rows_g = recv[:, width : 2 * width]
    rows_p = recv[:, 2 * width]
    near, far = shards[:-1], shards[-1]
    w_gate = jnp.stack([w[0] for w in near])
    w_up = jnp.stack([w[1] for w in near])
    w_down = jnp.stack([w[2] for w in near])
    sum_x, sum_p = stacked_terms(rows_x, rows_g, rows_p, w_gate, w_up, w_down)
    part_x, part_p = shard_terms(rows_x, rows_g, rows_p, *far)
    sum_x = (sum_x + part_x.astype(jnp.float32)).astype(jnp.bfloat16)
    sum_p = (sum_p + part_p.astype(jnp.float32)).astype(jnp.bfloat16)
    reply = jnp.concatenate([sum_x, pad_column(sum_p, groups * CAP)], axis=1)
    back = lax.all_to_all(
        reply.reshape(groups, CAP, -1), "ez", split_axis=0, concat_axis=0, tiled=True
    ).reshape(groups * CAP, -1)
    picked = jnp.take(back, place, axis=0)
    input_grad = jnp.sum(
        picked[:, :width].astype(jnp.float32).reshape(tok_count, TOPK, width), axis=1
    ).astype(jnp.bfloat16)
    gate_grad = picked[:, width].reshape(tok_count, TOPK)
    handed = from_behind(input_grad, "section", -1)
    return (handed[None], gate_grad[None])


def solution(mesh):
    sections = mesh.shape["section"]
    experts = mesh.shape["expert"]
    grid = mesh.devices.reshape(sections, experts // SPLIT, SPLIT)
    split_mesh = Mesh(grid, ("section", "ez", "ex"))
    spec3 = P("section", ("ez", "ex"), None)
    spec4 = P("section", ("ez", "ex"), None, None)
    in_specs = (spec3, spec3, spec3, spec3, spec4, spec4, spec4)
    out_specs = (spec3, spec3)
    return jax.shard_map(device_body, mesh=split_mesh, in_specs=in_specs, out_specs=out_specs, check_vma=False)
```

```python
import jax
import jax.numpy as jnp
from jax import lax
from jax.sharding import Mesh
from jax.sharding import PartitionSpec as P


SPLIT = 4
TOPK = 1
CAP = 16
PAD = 128


def from_behind(block, axis, distance):
    devices = range(lax.axis_size(axis))
    route = [((i - distance) % len(devices), i) for i in devices]
    return lax.ppermute(block, axis, route)


def ring_shift(block, axis, step):
    size = lax.axis_size(axis)
    return lax.ppermute(block, axis, [(i, (i + step) % size) for i in range(size)])


def gather_shards(weights, axis):
    left = [ring_shift(w, axis, 1) for w in weights]
    right = [ring_shift(w, axis, -1) for w in weights]
    opposite = []
    for a, b in zip(left, right):
        half = a.shape[0] // 2
        first = ring_shift(a[:half], axis, 1)
        second = ring_shift(b[half:], axis, -1)
        opposite.append(jnp.concatenate([first, second], axis=0))
    return [tuple(weights), tuple(left), tuple(right), tuple(opposite)]


def shard_terms(rows_x, rows_g, rows_p, w_gate, w_up, w_down):
    gate = jnp.dot(rows_x, w_gate, preferred_element_type=jnp.float32)
    upval = jnp.dot(rows_x, w_up, preferred_element_type=jnp.float32)
    sig = jax.nn.sigmoid(gate)
    act = gate * sig
    hidden = act * upval
    zeta = lax.dot_general(
        rows_g, w_down, (((1,), (1,)), ((), ())), preferred_element_type=jnp.float32
    )
    part_p = jnp.sum(hidden * zeta, axis=1).astype(jnp.bfloat16)
    d_hidden = rows_p.astype(jnp.float32)[:, None] * zeta
    d_gate = (d_hidden * upval * sig * (1.0 + gate * (1.0 - sig))).astype(jnp.bfloat16)
    d_up = (d_hidden * act).astype(jnp.bfloat16)
    part_x = lax.dot_general(
        d_gate, w_gate, (((1,), (1,)), ((), ())), preferred_element_type=jnp.float32
    )
    part_x = part_x + lax.dot_general(
        d_up, w_up, (((1,), (1,)), ((), ())), preferred_element_type=jnp.float32
    )
    return part_x.astype(jnp.bfloat16), part_p


def stacked_terms(rows_x, rows_g, rows_p, w_gate, w_up, w_down):
    gate = lax.dot_general(rows_x, w_gate, (((1,), (1,)), ((), ())), preferred_element_type=jnp.float32)
    upval = lax.dot_general(rows_x, w_up, (((1,), (1,)), ((), ())), preferred_element_type=jnp.float32)
    zeta = lax.dot_general(rows_g, w_down, (((1,), (2,)), ((), ())), preferred_element_type=jnp.float32)
    sig = jax.nn.sigmoid(gate)
    act = gate * sig
    hidden = act * upval
    part_p = jnp.sum(hidden * zeta, axis=2).astype(jnp.bfloat16)
    d_hidden = rows_p.astype(jnp.float32)[:, None, None] * zeta
    d_gate = (d_hidden * upval * sig * (1.0 + gate * (1.0 - sig))).astype(jnp.bfloat16)
    d_up = (d_hidden * act).astype(jnp.bfloat16)
    part_x = lax.dot_general(d_gate, w_gate, (((2,), (2,)), ((1,), (0,))), preferred_element_type=jnp.float32)
    part_x = part_x + lax.dot_general(d_up, w_up, (((2,), (2,)), ((1,), (0,))), preferred_element_type=jnp.float32)
    sum_x = jnp.sum(part_x.astype(jnp.bfloat16).astype(jnp.float32), axis=0)
    sum_p = jnp.sum(part_p.astype(jnp.float32), axis=1)
    return sum_x, sum_p


def pad_column(values, rows):
    col = jnp.zeros((rows, PAD), jnp.bfloat16)
    return col.at[:, 0].set(values.astype(jnp.bfloat16))


def device_body(tokens, grad_out, expert_ids, route_weight, gate_weight, up_weight, down_weight):
    feats = tokens[0]
    grads = grad_out[0]
    route_ids = expert_ids[0].reshape(-1)
    route_w = route_weight[0].reshape(-1)
    shards = gather_shards((gate_weight[0, 0], up_weight[0, 0], down_weight[0, 0]), "ex")
    groups = lax.axis_size("ez")
    tok_count, width = feats.shape
    rows = tok_count * TOPK
    onehot = (route_ids[:, None] == jnp.arange(groups, dtype=jnp.int32)[None, :]).astype(jnp.int32)
    before = jnp.cumsum(onehot, axis=0) - onehot
    slot = jnp.sum(before * onehot, axis=1)
    place = route_ids * CAP + slot
    table = (place[None, :] == jnp.arange(groups * CAP, dtype=jnp.int32)[:, None]).astype(
        jnp.bfloat16
    )
    packed = jnp.concatenate(
        [jnp.repeat(feats, TOPK, axis=0), jnp.repeat(grads, TOPK, axis=0), pad_column(route_w, rows)],
        axis=1,
    )
    send = jnp.dot(table, packed, preferred_element_type=jnp.float32).astype(jnp.bfloat16)
    recv = lax.all_to_all(
        send.reshape(groups, CAP, -1), "ez", split_axis=0, concat_axis=0, tiled=True
    ).reshape(groups * CAP, -1)
    rows_x = recv[:, :width]
    rows_g = recv[:, width : 2 * width]
    rows_p = recv[:, 2 * width]
    near, far = shards[:-1], shards[-1]
    w_gate = jnp.stack([w[0] for w in near])
    w_up = jnp.stack([w[1] for w in near])
    w_down = jnp.stack([w[2] for w in near])
    sum_x, sum_p = stacked_terms(rows_x, rows_g, rows_p, w_gate, w_up, w_down)
    part_x, part_p = shard_terms(rows_x, rows_g, rows_p, *far)
    sum_x = (sum_x + part_x.astype(jnp.float32)).astype(jnp.bfloat16)
    sum_p = (sum_p + part_p.astype(jnp.float32)).astype(jnp.bfloat16)
    reply = jnp.concatenate([sum_x, pad_column(sum_p, groups * CAP)], axis=1)
    back = lax.all_to_all(
        reply.reshape(groups, CAP, -1), "ez", split_axis=0, concat_axis=0, tiled=True
    ).reshape(groups * CAP, -1)
    picked = jnp.take(back, place, axis=0)
    input_grad = jnp.sum(
        picked[:, :width].astype(jnp.float32).reshape(tok_count, TOPK, width), axis=1
    ).astype(jnp.bfloat16)
    gate_grad = picked[:, width].reshape(tok_count, TOPK)
    handed = from_behind(input_grad, "section", -1)
    return (handed[None], gate_grad[None])


def solution(mesh):
    sections = mesh.shape["section"]
    experts = mesh.shape["expert"]
    grid = mesh.devices.reshape(sections, experts // SPLIT, SPLIT)
    split_mesh = Mesh(grid, ("section", "ez", "ex"))
    spec3 = P("section", ("ez", "ex"), None)
    spec4 = P("section", ("ez", "ex"), None, None)
    in_specs = (spec3, spec3, spec3, spec3, spec4, spec4, spec4)
    out_specs = (spec3, spec3)
    return jax.shard_map(device_body, mesh=split_mesh, in_specs=in_specs, out_specs=out_specs, check_vma=False)
```

```python
import jax
import jax.numpy as jnp
from jax import lax
from jax.sharding import Mesh
from jax.sharding import PartitionSpec as P


SPLIT = 4
TOPK = 1
CAP = 16
PAD = 128


def from_behind(block, axis, distance):
    devices = range(lax.axis_size(axis))
    route = [((i - distance) % len(devices), i) for i in devices]
    return lax.ppermute(block, axis, route)


def ring_shift(block, axis, step):
    size = lax.axis_size(axis)
    return lax.ppermute(block, axis, [(i, (i + step) % size) for i in range(size)])


def gather_shards(weights, axis):
    left = [ring_shift(w, axis, 1) for w in weights]
    right = [ring_shift(w, axis, -1) for w in weights]
    opposite = []
    for a, b, w in zip(left, right, weights):
        half = a.shape[0] // 2
        first = ring_shift(a[:half], axis, 1)
        second = ring_shift(b[half:], axis, -1)
        if w is weights[-1]:
            opposite.append(jnp.concatenate([first, second], axis=0))
        else:
            opposite.append((first, second))
    return [tuple(weights), tuple(left), tuple(right), tuple(opposite)]


def split_terms(rows_x, rows_g, rows_p, w_gate, w_up, w_down):
    half = w_gate[0].shape[0]

    def project(pair):
        low = jnp.dot(rows_x[:, :half], pair[0], preferred_element_type=jnp.float32)
        return low + jnp.dot(rows_x[:, half:], pair[1], preferred_element_type=jnp.float32)

    def back(d_val, pair, j):
        return lax.dot_general(
            d_val, pair[j], (((1,), (1,)), ((), ())), preferred_element_type=jnp.float32
        )

    gate = project(w_gate)
    upval = project(w_up)
    sig = jax.nn.sigmoid(gate)
    act = gate * sig
    hidden = act * upval
    zeta = lax.dot_general(
        rows_g, w_down, (((1,), (1,)), ((), ())), preferred_element_type=jnp.float32
    )
    part_p = jnp.sum(hidden * zeta, axis=1).astype(jnp.bfloat16)
    d_hidden = rows_p.astype(jnp.float32)[:, None] * zeta
    d_gate = (d_hidden * upval * sig * (1.0 + gate * (1.0 - sig))).astype(jnp.bfloat16)
    d_up = (d_hidden * act).astype(jnp.bfloat16)
    blocks = [back(d_gate, w_gate, j) + back(d_up, w_up, j) for j in range(2)]
    return jnp.concatenate(blocks, axis=1).astype(jnp.bfloat16), part_p


def stacked_terms(rows_x, rows_g, rows_p, w_gate, w_up, w_down):
    gate = lax.dot_general(rows_x, w_gate, (((1,), (1,)), ((), ())), preferred_element_type=jnp.float32)
    upval = lax.dot_general(rows_x, w_up, (((1,), (1,)), ((), ())), preferred_element_type=jnp.float32)
    zeta = lax.dot_general(rows_g, w_down, (((1,), (2,)), ((), ())), preferred_element_type=jnp.float32)
    sig = jax.nn.sigmoid(gate)
    act = gate * sig
    hidden = act * upval
    part_p = jnp.sum(hidden * zeta, axis=2).astype(jnp.bfloat16)
    d_hidden = rows_p.astype(jnp.float32)[:, None, None] * zeta
    d_gate = (d_hidden * upval * sig * (1.0 + gate * (1.0 - sig))).astype(jnp.bfloat16)
    d_up = (d_hidden * act).astype(jnp.bfloat16)
    part_x = lax.dot_general(d_gate, w_gate, (((2,), (2,)), ((1,), (0,))), preferred_element_type=jnp.float32)
    part_x = part_x + lax.dot_general(d_up, w_up, (((2,), (2,)), ((1,), (0,))), preferred_element_type=jnp.float32)
    sum_x = jnp.sum(part_x.astype(jnp.bfloat16).astype(jnp.float32), axis=0)
    sum_p = jnp.sum(part_p.astype(jnp.float32), axis=1)
    return sum_x, sum_p


def pad_column(values, rows):
    col = jnp.zeros((rows, PAD), jnp.bfloat16)
    return col.at[:, 0].set(values.astype(jnp.bfloat16))


def device_body(tokens, grad_out, expert_ids, route_weight, gate_weight, up_weight, down_weight):
    feats = tokens[0]
    grads = grad_out[0]
    route_ids = expert_ids[0].reshape(-1)
    route_w = route_weight[0].reshape(-1)
    shards = gather_shards((gate_weight[0, 0], up_weight[0, 0], down_weight[0, 0]), "ex")
    groups = lax.axis_size("ez")
    tok_count, width = feats.shape
    rows = tok_count * TOPK
    onehot = (route_ids[:, None] == jnp.arange(groups, dtype=jnp.int32)[None, :]).astype(jnp.int32)
    before = jnp.cumsum(onehot, axis=0) - onehot
    slot = jnp.sum(before * onehot, axis=1)
    place = route_ids * CAP + slot
    table = (place[None, :] == jnp.arange(groups * CAP, dtype=jnp.int32)[:, None]).astype(
        jnp.bfloat16
    )
    packed = jnp.concatenate(
        [jnp.repeat(feats, TOPK, axis=0), jnp.repeat(grads, TOPK, axis=0), pad_column(route_w, rows)],
        axis=1,
    )
    send = jnp.dot(table, packed, preferred_element_type=jnp.float32).astype(jnp.bfloat16)
    recv = lax.all_to_all(
        send.reshape(groups, CAP, -1), "ez", split_axis=0, concat_axis=0, tiled=True
    ).reshape(groups * CAP, -1)
    rows_x = recv[:, :width]
    rows_g = recv[:, width : 2 * width]
    rows_p = recv[:, 2 * width]
    near, far = shards[:-1], shards[-1]
    w_gate = jnp.stack([w[0] for w in near])
    w_up = jnp.stack([w[1] for w in near])
    w_down = jnp.stack([w[2] for w in near])
    sum_x, sum_p = stacked_terms(rows_x, rows_g, rows_p, w_gate, w_up, w_down)
    part_x, part_p = split_terms(rows_x, rows_g, rows_p, *far)
    sum_x = (sum_x + part_x.astype(jnp.float32)).astype(jnp.bfloat16)
    sum_p = (sum_p + part_p.astype(jnp.float32)).astype(jnp.bfloat16)
    reply = jnp.concatenate([sum_x, pad_column(sum_p, groups * CAP)], axis=1)
    back = lax.all_to_all(
        reply.reshape(groups, CAP, -1), "ez", split_axis=0, concat_axis=0, tiled=True
    ).reshape(groups * CAP, -1)
    picked = jnp.take(back, place, axis=0)
    input_grad = jnp.sum(
        picked[:, :width].astype(jnp.float32).reshape(tok_count, TOPK, width), axis=1
    ).astype(jnp.bfloat16)
    gate_grad = picked[:, width].reshape(tok_count, TOPK)
    handed = from_behind(input_grad, "section", -1)
    return (handed[None], gate_grad[None])


def solution(mesh):
    sections = mesh.shape["section"]
    experts = mesh.shape["expert"]
    grid = mesh.devices.reshape(sections, experts // SPLIT, SPLIT)
    split_mesh = Mesh(grid, ("section", "ez", "ex"))
    spec3 = P("section", ("ez", "ex"), None)
    spec4 = P("section", ("ez", "ex"), None, None)
    in_specs = (spec3, spec3, spec3, spec3, spec4, spec4, spec4)
    out_specs = (spec3, spec3)
    return jax.shard_map(device_body, mesh=split_mesh, in_specs=in_specs, out_specs=out_specs, check_vma=False)
```

```python
import jax
import jax.numpy as jnp
from jax import lax
from jax.sharding import Mesh
from jax.sharding import PartitionSpec as P


SPLIT = 4
TOPK = 1
CAP = 16
PAD = 128


def from_behind(block, axis, distance):
    devices = range(lax.axis_size(axis))
    route = [((i - distance) % len(devices), i) for i in devices]
    return lax.ppermute(block, axis, route)


def ring_shift(block, axis, step):
    size = lax.axis_size(axis)
    return lax.ppermute(block, axis, [(i, (i + step) % size) for i in range(size)])


def gather_shards(weights, axis):
    left = [ring_shift(w, axis, 1) for w in weights]
    right = [ring_shift(w, axis, -1) for w in weights]
    opposite = []
    for a, b in zip(left, right):
        half = a.shape[0] // 2
        first = ring_shift(a[:half], axis, 1)
        second = ring_shift(b[half:], axis, -1)
        opposite.append(jnp.concatenate([first, second], axis=0))
    return [tuple(weights), tuple(left), tuple(right), tuple(opposite)]


def shard_terms(rows_x, rows_g, rows_p, w_gate, w_up, w_down):
    gate = jnp.dot(rows_x, w_gate, preferred_element_type=jnp.float32)
    upval = jnp.dot(rows_x, w_up, preferred_element_type=jnp.float32)
    sig = jax.nn.sigmoid(gate)
    act = gate * sig
    hidden = act * upval
    zeta = lax.dot_general(
        rows_g, w_down, (((1,), (1,)), ((), ())), preferred_element_type=jnp.float32
    )
    part_p = jnp.sum(hidden * zeta, axis=1).astype(jnp.bfloat16)
    d_hidden = rows_p.astype(jnp.float32)[:, None] * zeta
    d_gate = (d_hidden * upval * sig * (1.0 + gate * (1.0 - sig))).astype(jnp.bfloat16)
    d_up = (d_hidden * act).astype(jnp.bfloat16)
    part_x = lax.dot_general(
        d_gate, w_gate, (((1,), (1,)), ((), ())), preferred_element_type=jnp.float32
    )
    part_x = part_x + lax.dot_general(
        d_up, w_up, (((1,), (1,)), ((), ())), preferred_element_type=jnp.float32
    )
    return part_x.astype(jnp.bfloat16), part_p


def stacked_terms(rows_x, rows_g, rows_p, w_gate, w_up, w_down):
    gate = lax.dot_general(rows_x, w_gate, (((1,), (1,)), ((), ())), preferred_element_type=jnp.float32)
    upval = lax.dot_general(rows_x, w_up, (((1,), (1,)), ((), ())), preferred_element_type=jnp.float32)
    zeta = lax.dot_general(rows_g, w_down, (((1,), (2,)), ((), ())), preferred_element_type=jnp.float32)
    sig = jax.nn.sigmoid(gate)
    act = gate * sig
    hidden = act * upval
    part_p = jnp.sum(hidden * zeta, axis=2).astype(jnp.bfloat16)
    d_hidden = rows_p.astype(jnp.float32)[:, None, None] * zeta
    d_gate = (d_hidden * upval * sig * (1.0 + gate * (1.0 - sig))).astype(jnp.bfloat16)
    d_up = (d_hidden * act).astype(jnp.bfloat16)
    part_x = lax.dot_general(d_gate, w_gate, (((2,), (2,)), ((1,), (0,))), preferred_element_type=jnp.float32)
    part_x = part_x + lax.dot_general(d_up, w_up, (((2,), (2,)), ((1,), (0,))), preferred_element_type=jnp.float32)
    sum_x = jnp.sum(part_x.astype(jnp.bfloat16).astype(jnp.float32), axis=0)
    sum_p = jnp.sum(part_p.astype(jnp.float32), axis=1)
    return sum_x, sum_p


def pad_column(values, rows):
    col = jnp.zeros((rows, PAD), jnp.bfloat16)
    return col.at[:, 0].set(values.astype(jnp.bfloat16))


def device_body(tokens, grad_out, expert_ids, route_weight, gate_weight, up_weight, down_weight):
    feats = tokens[0]
    grads = grad_out[0]
    route_ids = expert_ids[0].reshape(-1)
    route_w = route_weight[0].reshape(-1)
    shards = gather_shards((gate_weight[0, 0], up_weight[0, 0], down_weight[0, 0]), "ex")
    groups = lax.axis_size("ez")
    tok_count, width = feats.shape
    onehot = (route_ids[:, None] == jnp.arange(groups, dtype=jnp.int32)[None, :]).astype(jnp.int32)
    before = jnp.cumsum(onehot, axis=0) - onehot
    slot = jnp.sum(before * onehot, axis=1)
    place = route_ids * CAP + slot
    table = (place[None, :] == jnp.arange(groups * CAP, dtype=jnp.int32)[:, None]).astype(
        jnp.bfloat16
    )
    packed = jnp.concatenate(
        [jnp.repeat(feats, TOPK, axis=0), jnp.repeat(grads, TOPK, axis=0)],
        axis=1,
    )
    send = jnp.dot(table, packed, preferred_element_type=jnp.float32).astype(jnp.bfloat16)
    recv = lax.all_to_all(
        send.reshape(groups, CAP, -1), "ez", split_axis=0, concat_axis=0, tiled=True
    ).reshape(groups * CAP, -1)
    rows_x = recv[:, :width]
    rows_g = recv[:, width : 2 * width]
    rows_p = jnp.ones((recv.shape[0],), jnp.float32)
    near, far = shards[:-1], shards[-1]
    w_gate = jnp.stack([w[0] for w in near])
    w_up = jnp.stack([w[1] for w in near])
    w_down = jnp.stack([w[2] for w in near])
    sum_x, sum_p = stacked_terms(rows_x, rows_g, rows_p, w_gate, w_up, w_down)
    part_x, part_p = shard_terms(rows_x, rows_g, rows_p, *far)
    sum_x = (sum_x + part_x.astype(jnp.float32)).astype(jnp.bfloat16)
    sum_p = (sum_p + part_p.astype(jnp.float32)).astype(jnp.bfloat16)
    reply = jnp.concatenate([sum_x, pad_column(sum_p, groups * CAP)], axis=1)
    back = lax.all_to_all(
        reply.reshape(groups, CAP, -1), "ez", split_axis=0, concat_axis=0, tiled=True
    ).reshape(groups * CAP, -1)
    picked = jnp.take(back, place, axis=0)
    input_grad = jnp.sum(
        (route_w.astype(jnp.float32)[:, None] * picked[:, :width].astype(jnp.float32)).reshape(
            tok_count, TOPK, width
        ),
        axis=1,
    ).astype(jnp.bfloat16)
    gate_grad = picked[:, width].reshape(tok_count, TOPK)
    handed = from_behind(input_grad, "section", -1)
    return (handed[None], gate_grad[None])


def solution(mesh):
    sections = mesh.shape["section"]
    experts = mesh.shape["expert"]
    grid = mesh.devices.reshape(sections, experts // SPLIT, SPLIT)
    split_mesh = Mesh(grid, ("section", "ez", "ex"))
    spec3 = P("section", ("ez", "ex"), None)
    spec4 = P("section", ("ez", "ex"), None, None)
    in_specs = (spec3, spec3, spec3, spec3, spec4, spec4, spec4)
    out_specs = (spec3, spec3)
    return jax.shard_map(device_body, mesh=split_mesh, in_specs=in_specs, out_specs=out_specs, check_vma=False)
```
